128 devices in a mesh: grp: 4 (over z_hi, core), orb: 32 (over y, z_lo, x).
Axes of the slice: x: 4, y: 4, z: 4 (z_hi: 2, z_lo: 2; z = z_hi * 2 + z_lo), core: 2. Of those that a mesh axis runs over, the one named last changes fastest.
Arguments:
- df_panels: bfloat16 [128, 1024, 512], P(('grp', 'orb')), may hold values from -1.0546875 to 1.0546875
- occ_energy: float32 [128], replicated, may hold values from -2 to -0.5
- virt_energy: float32 [512], replicated, may hold values from 0.2 to 4
- fock_off: float32 [512, 512], replicated, may hold values from -0.25 to 0.25
- i_plan: int32 [3, 4], replicated, may hold values from 0 to 31
- pair_owner: int32 [1536, 1], P(('grp', 'orb')), may hold values from 0 to 3; in each aligned block of 12 rows (0 to 11, 12 to 23, ...) at most 4 rows name the same one
- pair_weight: float32 [1536], P(('grp', 'orb')), may hold values from -4 to 4
Outputs:
- residual: float32 [128, 512, 512], P(('grp', 'orb'))
The draws below stay inside these ranges and needn't reach their ends.
Inputs may be any that keep to these rules, and one draw needn't show every extreme that they name: `pair_owner`: each orbital's 12 rows name no group more than 4 times; some orbital names one group exactly 4 times.
All inputs are finite; a program needn't handle non-finite values.
Results may differ from the reference program's by a relative error of at most 0.0029.
Values may be sent and summed in bfloat16 or wider, within the bound.
No kernel may reach another device: no remote copies, remote signals or barrier semaphores. Data moves between devices by JAX's collectives and lax.ppermute only.
A program may use at most 128 MiB of HBM per device.

```python
import math
import jax
import jax.numpy as jnp
import numpy as np
from jax import lax

NAUX = 1024
NVIR = 512
STEPS = 3
CAP = 4
NO = 128
NT = 12
N_GRP = 4
N_ORB = 32


def set_ends(array, own_key, smallest, top_value):
    longest = array.shape.index(max(array.shape))
    spots = []
    for shift in (0, 1):
        where = [jax.random.randint(jax.random.fold_in(own_key, axis), (), 0, length) for axis, length in enumerate(array.shape)]
        where[longest] = (where[longest] + shift) % array.shape[longest]
        spots.append(tuple(where))
    return array.at[spots[0]].set(smallest).at[spots[1]].set(top_value)


def block_scale(stream_key, extent, pieces, least, largest):
    level = 1.0
    for axis_at, blocks in pieces:
        draws = jax.random.uniform(jax.random.fold_in(jax.random.fold_in(stream_key, 6), axis_at), (blocks,), jnp.float32, least / len(pieces), largest / len(pieces))
        level = level * jnp.repeat(jnp.exp(draws), extent[axis_at] // blocks).reshape((-1,) + (1,) * (len(extent) - 1 - axis_at))
    return level


def shared_out(own_key, own, number, rows, amount, top, limit, slope):
    sequence = jax.random.permutation(own_key, amount)
    crowded, common = shares(amount, rows * top, limit, slope, True), shares(amount, rows * top, limit, slope, False)
    places = jnp.arange(amount)

    def named(sizes, turn):
        used = int((sizes > 0).sum())
        fixed = max(1, used // 4)
        shifted = fixed + (places - fixed + turn * (used - fixed)) % max(1, amount - fixed)
        return jnp.zeros((amount,), jnp.int32).at[sequence[jnp.where(places < fixed, places, shifted)]].set(jnp.asarray(sizes, jnp.int32))

    sizes = jnp.where(number % 4 == 0, named(crowded, number // 4), named(common, number - number // 4 - 1))
    mixed = jax.random.permutation(jax.random.fold_in(own, 3), amount)
    source_of, receiver = mixed[0:amount // 2 * 2:2], mixed[1:amount // 2 * 2:2]
    room = jnp.minimum(sizes[source_of] - 1, limit - sizes[receiver]) // 2
    room = jnp.where((source_of == sequence[0]) | (receiver == sequence[0]) | (sizes[receiver] == 0), 0, jnp.maximum(room, 0))
    shifted = jax.random.randint(jax.random.fold_in(own, 4), (amount // 2,), 0, 1 << 20) % (room + 1)
    sizes = sizes.at[source_of].add(-shifted).at[receiver].add(shifted)
    items = jnp.searchsorted(jnp.cumsum(sizes), jnp.arange(rows * top), side="right").astype(jnp.int32)
    listing = items.reshape(top, rows).T
    listing = listing[jax.random.permutation(jax.random.fold_in(own, 1), rows)]
    turn = jax.random.randint(jax.random.fold_in(own, 2), (rows, 1), 0, top)
    return jnp.take_along_axis(listing, (jnp.arange(top)[None, :] + turn) % top, axis=1)


def shares(number_of, total, reach, skew, full):
    portions = [(1 << 20) // math.isqrt(standing ** skew) + 1 for standing in range(1, number_of + 1)]
    largest = reach if full else min(reach, max(-(-total // number_of), total * portions[0] // sum(portions)))
    least = 1 if total - largest >= number_of - 1 else 0
    counts, spare = [largest] + [least] * (number_of - 1), total - largest - least * (number_of - 1)
    while spare > 0:
        free = [i for i in range(1, number_of) if counts[i] < largest] or [i for i in range(1, number_of) if counts[i] < reach]
        mass, left = sum([portions[i] for i in free]), spare
        for i in free:
            more = min(reach - counts[i], max(1, left * portions[i] // mass), spare)
            counts[i] = counts[i] + more
            spare = spare - more
    return np.array(counts)


def centred(key, extent, deviation, most, split=(), kind=jnp.bfloat16):
    drawn = jax.random.normal(key, extent, jnp.float32) * deviation
    if len(split) > 0:
        drawn = block_scale(key, extent, split, -0.22, 0.18) * drawn
    return jnp.clip(drawn, min=-most, max=most).astype(kind)


def setup_inputs(seed: int = 0) -> dict:
    streams_of = jax.random.split(jax.random.key(seed), 8)
    df_panels = centred(streams_of[0], (NO, NAUX, NVIR), (NAUX ** -0.25), 1.0546875, ((0, 128),))
    occ_energy = jnp.clip(jax.random.uniform(streams_of[1], (NO,), jnp.float32, -2.0, -0.5), -2.0, -0.5)
    virt_energy = jnp.clip(jnp.exp(jax.random.uniform(streams_of[2], (NVIR,), jnp.float32, math.log(0.2), math.log(4.0))), 0.2, 4.0)
    fock_off = centred(streams_of[3], (NVIR, NVIR), NVIR ** -0.5, 0.25, (), jnp.float32)
    i_plan = set_ends(jax.random.randint(streams_of[4], (STEPS, N_GRP), 0, N_ORB), jax.random.fold_in(streams_of[4], 1), 0, N_ORB - 1).astype(jnp.int32)
    pair_owner_keys = jax.random.split(jax.random.fold_in(streams_of[5], 1), (NO * NT) // NT)
    pair_owner_turns = jax.random.permutation(jax.random.fold_in(streams_of[5], 3), (NO * NT) // NT)
    pair_owner = jax.vmap(lambda own, number: shared_out(jax.random.fold_in(streams_of[5], 2), own, number, NT, N_GRP, 1, CAP, 2))(pair_owner_keys, pair_owner_turns).reshape((NO * NT, 1))
    pair_weight = centred(streams_of[6], (NO * NT,), 1.0, 4.0, ((0, 128),), jnp.float32)
    return dict(df_panels=df_panels, occ_energy=occ_energy, virt_energy=virt_energy, fock_off=fock_off, i_plan=i_plan, pair_owner=pair_owner, pair_weight=pair_weight)


def reference(df_panels, occ_energy, virt_energy, fock_off, i_plan, pair_owner, pair_weight):
    highest = lax.Precision.HIGHEST
    panels_wide = df_panels.astype(jnp.float32)
    fock_matrix = jnp.diag(virt_energy) + 0.5 * (fock_off + fock_off.T)
    pair_sum = virt_energy[:, None] + virt_energy[None, :]
    groups_range = jnp.arange(N_GRP, dtype=jnp.int32)
    owners = pair_owner[:, 0].reshape(NO, NT)
    weights = pair_weight.reshape(NO, NT)

    def per_device(summed, device):
        own_panel = panels_wide[device]
        own_energy = occ_energy[device]
        tiles = []
        for step_index in range(STEPS):
            i_ids = (groups_range * N_ORB + i_plan[step_index]).astype(jnp.int32)
            integral = jnp.einsum("gxa,xb->gab", panels_wide[i_ids], own_panel, precision=highest)
            denominator = pair_sum[None] - occ_energy[i_ids][:, None, None] - own_energy
            tiles.append(integral / denominator)
        scaled = (jnp.concatenate(tiles, 0) * weights[device][:, None, None]).astype(jnp.bfloat16).astype(jnp.float32)
        one_hot = (owners[device][:, None] == groups_range[None, :]).astype(jnp.float32)
        partial_value = jnp.einsum("tg,tab->gab", one_hot, scaled, precision=highest)
        targets = (groups_range * N_ORB + device % N_ORB).astype(jnp.int32)
        return summed.at[targets].add(partial_value), None

    start = jnp.zeros((NO, NVIR, NVIR), jnp.float32)
    summed = lax.scan(per_device, start, jnp.arange(NO, dtype=jnp.int32))[0]
    left = jnp.einsum("ab,dbc->dac", fock_matrix, summed, precision=highest)
    right = jnp.einsum("dab,bc->dac", summed, fock_matrix, precision=highest)
    return left + right
```

```python
import jax
import jax.numpy as jnp
from jax import lax
from jax.sharding import PartitionSpec as P

NVIR = 512
STEPS = 3
CAP = 4


def shards(df_panels, occ_energy, virt_energy, fock_off, i_plan, pair_owner, pair_weight):
    highest = lax.Precision.HIGHEST
    group_count = lax.axis_size("grp")
    orbit_count = lax.axis_size("orb")
    my_group = lax.axis_index("grp")
    my_index = lax.axis_index("orb")
    my_orbital = my_group * orbit_count + my_index
    own_panel = df_panels[0]
    tile_count = STEPS * group_count

    groups_range = jnp.arange(group_count, dtype=jnp.int32)
    i_ids = (groups_range[None, :] * orbit_count + i_plan).reshape(tile_count)
    masked = jnp.where(
        (i_ids == my_orbital)[:, None, None], own_panel[None], jnp.zeros((), own_panel.dtype)
    )
    broadcast = lax.psum(masked, ("grp", "orb"))

    meta = jnp.concatenate([pair_weight, pair_owner[:, 0].astype(jnp.float32)])
    across = [(g, g ^ 2) for g in range(group_count)]
    beside = [(g, g ^ 1) for g in range(group_count)]
    far_panel = lax.ppermute(own_panel, "grp", across)
    far_meta = lax.ppermute(meta, "grp", across)
    near = lax.ppermute(jnp.stack([own_panel, far_panel]), "grp", beside)
    near_meta = lax.ppermute(jnp.stack([meta, far_meta]), "grp", beside)
    column = jnp.stack([own_panel, far_panel, near[0], near[1]])
    column_meta = jnp.stack([meta, far_meta, near_meta[0], near_meta[1]])
    source_groups = jnp.stack([my_group, my_group ^ 2, my_group ^ 1, my_group ^ 3])

    weights = column_meta[:, :tile_count]
    owners = column_meta[:, tile_count:]
    mine = owners == my_group.astype(jnp.float32)
    rank = jnp.cumsum(mine.astype(jnp.int32), axis=1) - 1
    slot_hit = mine[:, None, :] & (rank[:, None, :] == jnp.arange(CAP)[None, :, None])
    tile_range = jnp.arange(tile_count, dtype=jnp.int32)
    slot_tile = jnp.sum(jnp.where(slot_hit, tile_range, 0), axis=2)
    slot_weight = jnp.sum(jnp.where(slot_hit, weights[:, None, :], 0.0), axis=2)

    gathered = jnp.take(broadcast, slot_tile.reshape(-1), axis=0).reshape(
        group_count, CAP, *own_panel.shape
    )
    integral = jnp.einsum(
        "qkxa,qxb->qkab", gathered, column, preferred_element_type=jnp.float32
    )
    pair_sum = virt_energy[:, None] + virt_energy[None, :]
    i_energy = occ_energy[i_ids][slot_tile]
    j_energy = occ_energy[source_groups * orbit_count + my_index]
    denominator = (pair_sum[None, None] - i_energy[:, :, None, None]) - j_energy[:, None, None, None]
    amplitude = ((integral / denominator) * slot_weight[:, :, None, None]).astype(jnp.bfloat16)
    summed = jnp.sum(amplitude.astype(jnp.float32), axis=(0, 1))

    fock_matrix = jnp.diag(virt_energy) + 0.5 * (fock_off + fock_off.T)
    left = jnp.dot(fock_matrix, summed, precision=highest)
    right = jnp.dot(summed, fock_matrix, precision=highest)
    return (left + right)[None]


def solution(mesh):
    placed = (
        P(("grp", "orb"), None, None),
        P(),
        P(),
        P(),
        P(),
        P(("grp", "orb"), None),
        P(("grp", "orb")),
    )
    return jax.shard_map(
        shards, mesh=mesh, in_specs=placed, out_specs=P(("grp", "orb"), None, None), check_vma=False
    )
```

```python
import jax
import jax.numpy as jnp
from jax import lax
from jax.sharding import PartitionSpec as P

NVIR = 512
STEPS = 3
CAP = 4


def shards(df_panels, occ_energy, virt_energy, fock_off, i_plan, pair_owner, pair_weight):
    highest = lax.Precision.HIGHEST
    group_count = lax.axis_size("grp")
    orbit_count = lax.axis_size("orb")
    my_group = lax.axis_index("grp")
    my_index = lax.axis_index("orb")
    my_orbital = my_group * orbit_count + my_index
    own_panel = df_panels[0]
    tile_count = STEPS * group_count

    groups_range = jnp.arange(group_count, dtype=jnp.int32)
    i_ids = (groups_range[None, :] * orbit_count + i_plan).reshape(tile_count)
    own_turned = own_panel.T
    masked = jnp.where(
        (i_ids == my_orbital)[:, None, None], own_turned[None], jnp.zeros((), own_panel.dtype)
    )
    broadcast = lax.psum(masked, ("grp", "orb"))

    meta = jnp.concatenate([pair_weight, pair_owner[:, 0].astype(jnp.float32)])
    across = [(g, g ^ 2) for g in range(group_count)]
    beside = [(g, g ^ 1) for g in range(group_count)]
    far_panel = lax.ppermute(own_panel, "grp", across)
    far_meta = lax.ppermute(meta, "grp", across)
    near = lax.ppermute(jnp.stack([own_panel, far_panel]), "grp", beside)
    near_meta = lax.ppermute(jnp.stack([meta, far_meta]), "grp", beside)
    column = jnp.stack([own_panel, far_panel, near[0], near[1]])
    column_meta = jnp.stack([meta, far_meta, near_meta[0], near_meta[1]])
    source_groups = jnp.stack([my_group, my_group ^ 2, my_group ^ 1, my_group ^ 3])

    weights = column_meta[:, :tile_count]
    owners = column_meta[:, tile_count:]
    mine = owners == my_group.astype(jnp.float32)
    rank = jnp.cumsum(mine.astype(jnp.int32), axis=1) - 1
    slot_hit = mine[:, None, :] & (rank[:, None, :] == jnp.arange(CAP)[None, :, None])
    tile_range = jnp.arange(tile_count, dtype=jnp.int32)
    slot_tile = jnp.sum(jnp.where(slot_hit, tile_range, 0), axis=2)
    slot_weight = jnp.sum(jnp.where(slot_hit, weights[:, None, :], 0.0), axis=2)

    pair_sum = virt_energy[:, None] + virt_energy[None, :]
    i_energy = occ_energy[i_ids][slot_tile]
    j_energy = occ_energy[source_groups * orbit_count + my_index]
    summed = jnp.zeros((NVIR, NVIR), jnp.float32)
    for q in range(group_count):
        for k in range(CAP):
            left_panel = lax.dynamic_index_in_dim(broadcast, slot_tile[q, k], 0, keepdims=False)
            integral = jnp.dot(left_panel, column[q], preferred_element_type=jnp.float32)
            denominator = (pair_sum - i_energy[q, k]) - j_energy[q]
            amplitude = ((integral / denominator) * slot_weight[q, k]).astype(jnp.bfloat16)
            summed = summed + amplitude.astype(jnp.float32)

    fock_matrix = jnp.diag(virt_energy) + 0.5 * (fock_off + fock_off.T)
    left = jnp.dot(fock_matrix, summed, precision=highest)
    right = jnp.dot(summed, fock_matrix, precision=highest)
    return (left + right)[None]


def solution(mesh):
    placed = (
        P(("grp", "orb"), None, None),
        P(),
        P(),
        P(),
        P(),
        P(("grp", "orb"), None),
        P(("grp", "orb")),
    )
    return jax.shard_map(
        shards, mesh=mesh, in_specs=placed, out_specs=P(("grp", "orb"), None, None), check_vma=False
    )
```

```python
import jax
import jax.numpy as jnp
from jax import lax
from jax.sharding import PartitionSpec as P
from jax.experimental import pallas as pl
from jax.experimental.pallas import tpu as pltpu

NVIR = 512
STEPS = 3
CAP = 4


def slot_kernel(tiles_ref, scalars_ref, left_ref, right_ref, pair_ref, out_ref):
    step = pl.program_id(0)
    slots = pl.num_programs(0)
    integral = jnp.dot(left_ref[...], right_ref[...], preferred_element_type=jnp.float32)
    denominator = (pair_ref[...] - scalars_ref[step]) - scalars_ref[slots + step]
    amplitude = ((integral / denominator) * scalars_ref[2 * slots + step]).astype(jnp.bfloat16)

    @pl.when(step == 0)
    def _():
        out_ref[...] = amplitude.astype(jnp.float32)

    @pl.when(step > 0)
    def _():
        out_ref[...] += amplitude.astype(jnp.float32)


def summed_tiles(slot_tile, scalars, broadcast, column, pair_sum):
    slots = slot_tile.shape[0]
    per_source = slots // column.shape[0]
    _, rows, depth = broadcast.shape
    grid_spec = pltpu.PrefetchScalarGridSpec(
        num_scalar_prefetch=1,
        grid=(slots,),
        in_specs=[
            pl.BlockSpec(memory_space=pltpu.SMEM),
            pl.BlockSpec((None, rows, depth), lambda s, tiles: (tiles[s], 0, 0)),
            pl.BlockSpec((None, depth, rows), lambda s, tiles: (s // per_source, 0, 0)),
            pl.BlockSpec((rows, rows), lambda s, tiles: (0, 0)),
        ],
        out_specs=pl.BlockSpec((rows, rows), lambda s, tiles: (0, 0)),
    )
    return pl.pallas_call(
        slot_kernel,
        grid_spec=grid_spec,
        out_shape=jax.ShapeDtypeStruct((rows, rows), jnp.float32),
        compiler_params=pltpu.CompilerParams(dimension_semantics=("arbitrary",)),
    )(slot_tile, scalars, broadcast, column, pair_sum)


def shards(df_panels, occ_energy, virt_energy, fock_off, i_plan, pair_owner, pair_weight):
    highest = lax.Precision.HIGHEST
    group_count = lax.axis_size("grp")
    orbit_count = lax.axis_size("orb")
    my_group = lax.axis_index("grp")
    my_index = lax.axis_index("orb")
    my_orbital = my_group * orbit_count + my_index
    own_panel = df_panels[0]
    tile_count = STEPS * group_count

    groups_range = jnp.arange(group_count, dtype=jnp.int32)
    i_ids = (groups_range[None, :] * orbit_count + i_plan).reshape(tile_count)
    own_turned = own_panel.T
    masked = jnp.where(
        (i_ids == my_orbital)[:, None, None], own_turned[None], jnp.zeros((), own_panel.dtype)
    )
    broadcast = lax.psum(masked, ("grp", "orb"))

    meta = jnp.concatenate([pair_weight, pair_owner[:, 0].astype(jnp.float32)])
    across = [(g, g ^ 2) for g in range(group_count)]
    beside = [(g, g ^ 1) for g in range(group_count)]
    far_panel = lax.ppermute(own_panel, "grp", across)
    far_meta = lax.ppermute(meta, "grp", across)
    near = lax.ppermute(jnp.stack([own_panel, far_panel]), "grp", beside)
    near_meta = lax.ppermute(jnp.stack([meta, far_meta]), "grp", beside)
    column = jnp.stack([own_panel, far_panel, near[0], near[1]])
    column_meta = jnp.stack([meta, far_meta, near_meta[0], near_meta[1]])
    source_groups = jnp.stack([my_group, my_group ^ 2, my_group ^ 1, my_group ^ 3])

    weights = column_meta[:, :tile_count]
    owners = column_meta[:, tile_count:]
    mine = owners == my_group.astype(jnp.float32)
    rank = jnp.cumsum(mine.astype(jnp.int32), axis=1) - 1
    slot_hit = mine[:, None, :] & (rank[:, None, :] == jnp.arange(CAP)[None, :, None])
    tile_range = jnp.arange(tile_count, dtype=jnp.int32)
    slot_tile = jnp.sum(jnp.where(slot_hit, tile_range, 0), axis=2)
    slot_weight = jnp.sum(jnp.where(slot_hit, weights[:, None, :], 0.0), axis=2)

    pair_sum = virt_energy[:, None] + virt_energy[None, :]
    i_energy = occ_energy[i_ids][slot_tile]
    j_energy = occ_energy[source_groups * orbit_count + my_index]
    scalars = jnp.concatenate(
        [
            i_energy.reshape(-1),
            jnp.repeat(j_energy, CAP),
            slot_weight.reshape(-1),
        ]
    )
    summed = summed_tiles(slot_tile.reshape(-1), scalars, broadcast, column, pair_sum)

    fock_matrix = jnp.diag(virt_energy) + 0.5 * (fock_off + fock_off.T)
    left = jnp.dot(fock_matrix, summed, precision=highest)
    right = jnp.dot(summed, fock_matrix, precision=highest)
    return (left + right)[None]


def solution(mesh):
    placed = (
        P(("grp", "orb"), None, None),
        P(),
        P(),
        P(),
        P(),
        P(("grp", "orb"), None),
        P(("grp", "orb")),
    )
    return jax.shard_map(
        shards, mesh=mesh, in_specs=placed, out_specs=P(("grp", "orb"), None, None), check_vma=False
    )
```

```python
import jax
import jax.numpy as jnp
from jax import lax
from jax.sharding import Mesh, PartitionSpec as P
from jax.experimental import pallas as pl
from jax.experimental.pallas import tpu as pltpu

NVIR = 512
STEPS = 3
CAP = 4


def slot_kernel(tiles_ref, scalars_ref, left_ref, right_ref, pair_ref, out_ref):
    step = pl.program_id(0)
    slots = pl.num_programs(0)
    integral = jnp.dot(left_ref[...], right_ref[...], preferred_element_type=jnp.float32)
    denominator = (pair_ref[...] - scalars_ref[step]) - scalars_ref[slots + step]
    amplitude = ((integral / denominator) * scalars_ref[2 * slots + step]).astype(jnp.bfloat16)

    @pl.when(step == 0)
    def _():
        out_ref[...] = amplitude.astype(jnp.float32)

    @pl.when(step > 0)
    def _():
        out_ref[...] += amplitude.astype(jnp.float32)


def summed_tiles(slot_tile, scalars, broadcast, column, pair_sum):
    slots = slot_tile.shape[0]
    per_source = slots // column.shape[0]
    _, rows, depth = broadcast.shape
    grid_spec = pltpu.PrefetchScalarGridSpec(
        num_scalar_prefetch=1,
        grid=(slots,),
        in_specs=[
            pl.BlockSpec(memory_space=pltpu.SMEM),
            pl.BlockSpec((None, rows, depth), lambda s, tiles: (tiles[s], 0, 0)),
            pl.BlockSpec((None, depth, rows), lambda s, tiles: (s // per_source, 0, 0)),
            pl.BlockSpec((rows, rows), lambda s, tiles: (0, 0)),
        ],
        out_specs=pl.BlockSpec((rows, rows), lambda s, tiles: (0, 0)),
    )
    return pl.pallas_call(
        slot_kernel,
        grid_spec=grid_spec,
        out_shape=jax.ShapeDtypeStruct((rows, rows), jnp.float32),
        compiler_params=pltpu.CompilerParams(dimension_semantics=("arbitrary",)),
    )(slot_tile, scalars, broadcast, column, pair_sum)


def shards(df_panels, occ_energy, virt_energy, fock_off, i_plan, pair_owner, pair_weight):
    highest = lax.Precision.HIGHEST
    halves = lax.axis_size("zh")
    cores = lax.axis_size("core")
    group_count = halves * cores
    orbit_count = lax.axis_size("orb")
    my_core = lax.axis_index("core")
    my_group = lax.axis_index("zh") * cores + my_core
    my_index = lax.axis_index("orb")
    my_orbital = my_group * orbit_count + my_index
    own_panel = df_panels[0]
    tile_count = STEPS * group_count

    groups_range = jnp.arange(group_count, dtype=jnp.int32)
    i_ids = (groups_range[None, :] * orbit_count + i_plan).reshape(tile_count)
    own_turned = own_panel.T
    core_ids = lax.dynamic_index_in_dim(
        i_ids.reshape(STEPS, halves, cores), my_core, axis=2, keepdims=False
    ).reshape(-1)
    masked = jnp.where(
        (core_ids == my_orbital)[:, None, None], own_turned[None], jnp.zeros((), own_panel.dtype)
    )
    mine = lax.psum(masked, ("zh", "orb"))
    theirs = lax.ppermute(mine, "core", [(c, c ^ 1) for c in range(cores)])
    broadcast = jnp.concatenate([mine, theirs])

    meta = jnp.concatenate([pair_weight, pair_owner[:, 0].astype(jnp.float32)])
    across = [(z, z ^ 1) for z in range(halves)]
    beside = [(c, c ^ 1) for c in range(cores)]
    far_panel = lax.ppermute(own_panel, "zh", across)
    far_meta = lax.ppermute(meta, "zh", across)
    near = lax.ppermute(jnp.stack([own_panel, far_panel]), "core", beside)
    near_meta = lax.ppermute(jnp.stack([meta, far_meta]), "core", beside)
    column = jnp.stack([own_panel, far_panel, near[0], near[1]])
    column_meta = jnp.stack([meta, far_meta, near_meta[0], near_meta[1]])
    source_groups = jnp.stack([my_group, my_group ^ 2, my_group ^ 1, my_group ^ 3])

    weights = column_meta[:, :tile_count]
    owners = column_meta[:, tile_count:]
    mine = owners == my_group.astype(jnp.float32)
    rank = jnp.cumsum(mine.astype(jnp.int32), axis=1) - 1
    slot_hit = mine[:, None, :] & (rank[:, None, :] == jnp.arange(CAP)[None, :, None])
    tile_range = jnp.arange(tile_count, dtype=jnp.int32)
    slot_tile = jnp.sum(jnp.where(slot_hit, tile_range, 0), axis=2)
    slot_weight = jnp.sum(jnp.where(slot_hit, weights[:, None, :], 0.0), axis=2)

    pair_sum = virt_energy[:, None] + virt_energy[None, :]
    i_energy = occ_energy[i_ids][slot_tile]
    j_energy = occ_energy[source_groups * orbit_count + my_index]
    scalars = jnp.concatenate(
        [
            i_energy.reshape(-1),
            jnp.repeat(j_energy, CAP),
            slot_weight.reshape(-1),
        ]
    )
    step_of, group_of = slot_tile // group_count, slot_tile % group_count
    position = (
        jnp.where(group_of % cores == my_core, 0, tile_count // cores)
        + step_of * halves
        + group_of // cores
    )
    summed = summed_tiles(position.reshape(-1), scalars, broadcast, column, pair_sum)

    fock_matrix = jnp.diag(virt_energy) + 0.5 * (fock_off + fock_off.T)
    left = jnp.dot(fock_matrix, summed, precision=highest)
    right = jnp.dot(summed, fock_matrix, precision=highest)
    return (left + right)[None]


def solution(mesh):
    group_count, orbit_count = mesh.devices.shape
    split = Mesh(mesh.devices.reshape(2, group_count // 2, orbit_count), ("zh", "core", "orb"))
    spread = ("zh", "core", "orb")
    placed = (
        P(spread, None, None),
        P(),
        P(),
        P(),
        P(),
        P(spread, None),
        P(spread),
    )
    return jax.shard_map(
        shards, mesh=split, in_specs=placed, out_specs=P(spread, None, None), check_vma=False
    )
```

```python
import jax
import jax.numpy as jnp
from jax import lax
from jax.sharding import Mesh, PartitionSpec as P
from jax.experimental import pallas as pl
from jax.experimental.pallas import tpu as pltpu

STEPS = 3
CAP = 4


def slot_kernel(tiles_ref, scalars_ref, mine_ref, theirs_ref, right_ref, pair_ref, out_ref):
    step = pl.program_id(0)
    slots = pl.num_programs(0)

    def accumulate(left_ref):
        integral = jnp.dot(left_ref[...], right_ref[...], preferred_element_type=jnp.float32)
        denominator = (pair_ref[...] - scalars_ref[step]) - scalars_ref[slots + step]
        amplitude = ((integral / denominator) * scalars_ref[2 * slots + step]).astype(jnp.bfloat16)

        @pl.when(step == 0)
        def _():
            out_ref[...] = amplitude.astype(jnp.float32)

        @pl.when(step > 0)
        def _():
            out_ref[...] += amplitude.astype(jnp.float32)

    @pl.when(tiles_ref[step] == 0)
    def _():
        accumulate(mine_ref)

    @pl.when(tiles_ref[step] != 0)
    def _():
        accumulate(theirs_ref)


def held_index(present, local):
    steps = jnp.arange(present.shape[0], dtype=jnp.int32)
    last = lax.cummax(jnp.where(present, steps, -1))
    first = jnp.argmax(present)
    return jnp.where(last >= 0, local[jnp.maximum(last, 0)], local[first])


def summed_tiles(position, scalars, mine, theirs, column, pair_sum):
    slots = position.shape[0]
    per_source = slots // column.shape[0]
    half, rows, depth = mine.shape
    in_theirs = position >= half
    local = position % half
    tables = jnp.concatenate(
        [
            in_theirs.astype(jnp.int32),
            held_index(~in_theirs, local),
            held_index(in_theirs, local),
        ]
    )
    grid_spec = pltpu.PrefetchScalarGridSpec(
        num_scalar_prefetch=1,
        grid=(slots,),
        in_specs=[
            pl.BlockSpec(memory_space=pltpu.SMEM),
            pl.BlockSpec((None, rows, depth), lambda s, tiles: (tiles[slots + s], 0, 0)),
            pl.BlockSpec((None, rows, depth), lambda s, tiles: (tiles[2 * slots + s], 0, 0)),
            pl.BlockSpec((None, depth, rows), lambda s, tiles: (s // per_source, 0, 0)),
            pl.BlockSpec((rows, rows), lambda s, tiles: (0, 0)),
        ],
        out_specs=pl.BlockSpec((rows, rows), lambda s, tiles: (0, 0)),
    )
    return pl.pallas_call(
        slot_kernel,
        grid_spec=grid_spec,
        out_shape=jax.ShapeDtypeStruct((rows, rows), jnp.float32),
        compiler_params=pltpu.CompilerParams(dimension_semantics=("arbitrary",)),
    )(tables, scalars, mine, theirs, column, pair_sum)


def layer(df_panels, occ_energy, virt_energy, fock_off, i_plan, pair_owner, pair_weight):
    highest = lax.Precision.HIGHEST
    halves = lax.axis_size("zh")
    cores = lax.axis_size("core")
    group_count = halves * cores
    orbit_count = lax.axis_size("orb")
    my_core = lax.axis_index("core")
    my_group = lax.axis_index("zh") * cores + my_core
    my_index = lax.axis_index("orb")
    my_orbital = my_group * orbit_count + my_index
    own_panel = df_panels[0]
    tile_count = STEPS * group_count

    groups_range = jnp.arange(group_count, dtype=jnp.int32)
    i_ids = (groups_range[None, :] * orbit_count + i_plan).reshape(tile_count)
    own_turned = own_panel.T
    core_ids = lax.dynamic_index_in_dim(
        i_ids.reshape(STEPS, halves, cores), my_core, axis=2, keepdims=False
    ).reshape(-1)
    masked = jnp.where(
        (core_ids == my_orbital)[:, None, None], own_turned[None], jnp.zeros((), own_panel.dtype)
    )
    own_half = lax.psum(masked, ("zh", "orb"))
    other_half = lax.ppermute(own_half, "core", [(c, c ^ 1) for c in range(cores)])

    meta = jnp.concatenate([pair_weight, pair_owner[:, 0].astype(jnp.float32)])
    across = [(z, z ^ 1) for z in range(halves)]
    beside = [(c, c ^ 1) for c in range(cores)]
    far_panel = lax.ppermute(own_panel, "zh", across)
    far_meta = lax.ppermute(meta, "zh", across)
    near = lax.ppermute(jnp.stack([own_panel, far_panel]), "core", beside)
    near_meta = lax.ppermute(jnp.stack([meta, far_meta]), "core", beside)
    column = jnp.stack([own_panel, far_panel, near[0], near[1]])
    column_meta = jnp.stack([meta, far_meta, near_meta[0], near_meta[1]])
    source_groups = jnp.stack([my_group, my_group ^ 2, my_group ^ 1, my_group ^ 3])

    weights = column_meta[:, :tile_count]
    owners = column_meta[:, tile_count:]
    mine = owners == my_group.astype(jnp.float32)
    rank = jnp.cumsum(mine.astype(jnp.int32), axis=1) - 1
    slot_hit = mine[:, None, :] & (rank[:, None, :] == jnp.arange(CAP)[None, :, None])
    tile_range = jnp.arange(tile_count, dtype=jnp.int32)
    slot_tile = jnp.sum(jnp.where(slot_hit, tile_range, 0), axis=2)
    slot_weight = jnp.sum(jnp.where(slot_hit, weights[:, None, :], 0.0), axis=2)

    pair_sum = virt_energy[:, None] + virt_energy[None, :]
    i_energy = occ_energy[i_ids][slot_tile]
    j_energy = occ_energy[source_groups * orbit_count + my_index]
    scalars = jnp.concatenate(
        [
            i_energy.reshape(-1),
            jnp.repeat(j_energy, CAP),
            slot_weight.reshape(-1),
        ]
    )
    step_of, group_of = slot_tile // group_count, slot_tile % group_count
    position = (
        jnp.where(group_of % cores == my_core, 0, tile_count // cores)
        + step_of * halves
        + group_of // cores
    )
    summed = summed_tiles(position.reshape(-1), scalars, own_half, other_half, column, pair_sum)

    fock_matrix = jnp.diag(virt_energy) + 0.5 * (fock_off + fock_off.T)
    left = jnp.dot(fock_matrix, summed, precision=highest)
    right = jnp.dot(summed, fock_matrix, precision=highest)
    return (left + right)[None]


def solution(mesh):
    group_count, orbit_count = mesh.devices.shape
    split = Mesh(mesh.devices.reshape(2, group_count // 2, orbit_count), ("zh", "core", "orb"))
    spread = ("zh", "core", "orb")
    placed = (
        P(spread, None, None),
        P(),
        P(),
        P(),
        P(),
        P(spread, None),
        P(spread),
    )
    return jax.shard_map(
        layer, mesh=split, in_specs=placed, out_specs=P(spread, None, None), check_vma=False
    )
```

```python
import jax
import jax.numpy as jnp
from jax import lax
from jax.sharding import Mesh, PartitionSpec as P
from jax.experimental import pallas as pl
from jax.experimental.pallas import tpu as pltpu

STEPS = 3
CAP = 4


def amplitude_of(step, slots, scalars_ref, left_ref, right_ref, pair_ref):
    integral = jnp.dot(left_ref[...], right_ref[...], preferred_element_type=jnp.float32)
    denominator = (pair_ref[...] - scalars_ref[step]) - scalars_ref[slots + step]
    amplitude = ((integral / denominator) * scalars_ref[2 * slots + step]).astype(jnp.bfloat16)
    return amplitude.astype(jnp.float32)


def own_kernel(tiles_ref, scalars_ref, left_ref, right_ref, pair_ref, out_ref):
    step = pl.program_id(0)
    slots = pl.num_programs(0)

    @pl.when(step == 0)
    def _():
        out_ref[...] = jnp.zeros(out_ref.shape, out_ref.dtype)

    @pl.when(tiles_ref[step] == 0)
    def _():
        out_ref[...] += amplitude_of(step, slots, scalars_ref, left_ref, right_ref, pair_ref)


def other_kernel(tiles_ref, scalars_ref, left_ref, right_ref, pair_ref, acc_ref, out_ref):
    step = pl.program_id(0)
    slots = pl.num_programs(0)

    @pl.when(step == 0)
    def _():
        out_ref[...] = acc_ref[...]

    @pl.when(tiles_ref[step] != 0)
    def _():
        out_ref[...] += amplitude_of(step, slots, scalars_ref, left_ref, right_ref, pair_ref)


def held_index(present, local):
    steps = jnp.arange(present.shape[0], dtype=jnp.int32)
    last = lax.cummax(jnp.where(present, steps, -1))
    first = jnp.argmax(present)
    return jnp.where(last >= 0, local[jnp.maximum(last, 0)], local[first])


def summed_tiles(position, scalars, mine, theirs, column, pair_sum):
    slots = position.shape[0]
    per_source = slots // column.shape[0]
    half, rows, depth = mine.shape
    in_theirs = position >= half
    local = position % half
    tables = jnp.concatenate(
        [in_theirs.astype(jnp.int32), held_index(~in_theirs, local), held_index(in_theirs, local)]
    )

    def specs(offset, extra):
        return pltpu.PrefetchScalarGridSpec(
            num_scalar_prefetch=1,
            grid=(slots,),
            in_specs=[
                pl.BlockSpec(memory_space=pltpu.SMEM),
                pl.BlockSpec((None, rows, depth), lambda s, tiles: (tiles[offset + s], 0, 0)),
                pl.BlockSpec((None, depth, rows), lambda s, tiles: (s // per_source, 0, 0)),
                pl.BlockSpec((rows, rows), lambda s, tiles: (0, 0)),
            ]
            + [pl.BlockSpec((rows, rows), lambda s, tiles: (0, 0))] * extra,
            out_specs=pl.BlockSpec((rows, rows), lambda s, tiles: (0, 0)),
        )

    params = pltpu.CompilerParams(dimension_semantics=("arbitrary",))
    out_shape = jax.ShapeDtypeStruct((rows, rows), jnp.float32)
    partial = pl.pallas_call(
        own_kernel, grid_spec=specs(slots, 0), out_shape=out_shape, compiler_params=params
    )(tables, scalars, mine, column, pair_sum)
    return pl.pallas_call(
        other_kernel,
        grid_spec=specs(2 * slots, 1),
        out_shape=out_shape,
        compiler_params=params,
        input_output_aliases={5: 0},
    )(tables, scalars, theirs, column, pair_sum, partial)


def layer(df_panels, occ_energy, virt_energy, fock_off, i_plan, pair_owner, pair_weight):
    highest = lax.Precision.HIGHEST
    halves = lax.axis_size("zh")
    cores = lax.axis_size("core")
    group_count = halves * cores
    orbit_count = lax.axis_size("orb")
    my_core = lax.axis_index("core")
    my_group = lax.axis_index("zh") * cores + my_core
    my_index = lax.axis_index("orb")
    my_orbital = my_group * orbit_count + my_index
    own_panel = df_panels[0]
    tile_count = STEPS * group_count

    groups_range = jnp.arange(group_count, dtype=jnp.int32)
    i_ids = (groups_range[None, :] * orbit_count + i_plan).reshape(tile_count)
    own_turned = own_panel.T
    core_ids = lax.dynamic_index_in_dim(
        i_ids.reshape(STEPS, halves, cores), my_core, axis=2, keepdims=False
    ).reshape(-1)
    masked = jnp.where(
        (core_ids == my_orbital)[:, None, None], own_turned[None], jnp.zeros((), own_panel.dtype)
    )
    own_half = lax.psum(masked, ("zh", "orb"))
    other_half = lax.ppermute(own_half, "core", [(c, c ^ 1) for c in range(cores)])

    meta = jnp.concatenate([pair_weight, pair_owner[:, 0].astype(jnp.float32)])
    across = [(z, z ^ 1) for z in range(halves)]
    beside = [(c, c ^ 1) for c in range(cores)]
    far_panel = lax.ppermute(own_panel, "zh", across)
    far_meta = lax.ppermute(meta, "zh", across)
    near = lax.ppermute(jnp.stack([own_panel, far_panel]), "core", beside)
    near_meta = lax.ppermute(jnp.stack([meta, far_meta]), "core", beside)
    column = jnp.stack([own_panel, far_panel, near[0], near[1]])
    column_meta = jnp.stack([meta, far_meta, near_meta[0], near_meta[1]])
    source_groups = jnp.stack([my_group, my_group ^ 2, my_group ^ 1, my_group ^ 3])

    weights = column_meta[:, :tile_count]
    owners = column_meta[:, tile_count:]
    mine = owners == my_group.astype(jnp.float32)
    rank = jnp.cumsum(mine.astype(jnp.int32), axis=1) - 1
    slot_hit = mine[:, None, :] & (rank[:, None, :] == jnp.arange(CAP)[None, :, None])
    tile_range = jnp.arange(tile_count, dtype=jnp.int32)
    slot_tile = jnp.sum(jnp.where(slot_hit, tile_range, 0), axis=2)
    slot_weight = jnp.sum(jnp.where(slot_hit, weights[:, None, :], 0.0), axis=2)

    pair_sum = virt_energy[:, None] + virt_energy[None, :]
    i_energy = occ_energy[i_ids][slot_tile]
    j_energy = occ_energy[source_groups * orbit_count + my_index]
    scalars = jnp.concatenate(
        [
            i_energy.reshape(-1),
            jnp.repeat(j_energy, CAP),
            slot_weight.reshape(-1),
        ]
    )
    step_of, group_of = slot_tile // group_count, slot_tile % group_count
    position = (
        jnp.where(group_of % cores == my_core, 0, tile_count // cores)
        + step_of * halves
        + group_of // cores
    )
    summed = summed_tiles(position.reshape(-1), scalars, own_half, other_half, column, pair_sum)

    fock_matrix = jnp.diag(virt_energy) + 0.5 * (fock_off + fock_off.T)
    left = jnp.dot(fock_matrix, summed, precision=highest)
    right = jnp.dot(summed, fock_matrix, precision=highest)
    return (left + right)[None]


def solution(mesh):
    group_count, orbit_count = mesh.devices.shape
    split = Mesh(mesh.devices.reshape(2, group_count // 2, orbit_count), ("zh", "core", "orb"))
    spread = ("zh", "core", "orb")
    placed = (
        P(spread, None, None),
        P(),
        P(),
        P(),
        P(),
        P(spread, None),
        P(spread),
    )
    return jax.shard_map(
        layer, mesh=split, in_specs=placed, out_specs=P(spread, None, None), check_vma=False
    )
```

```python
import jax
import jax.numpy as jnp
from jax import lax
from jax.sharding import Mesh, PartitionSpec as P
from jax.experimental import pallas as pl
from jax.experimental.pallas import tpu as pltpu

STEPS = 3
CAP = 4


def slot_kernel(tiles_ref, scalars_ref, mine_ref, theirs_ref, right_ref, pair_ref, out_ref):
    step = pl.program_id(0)
    slots = pl.num_programs(0)

    def accumulate(left_ref):
        integral = jnp.dot(left_ref[...], right_ref[...], preferred_element_type=jnp.float32)
        denominator = (pair_ref[...] - scalars_ref[step]) - scalars_ref[slots + step]
        amplitude = ((integral / denominator) * scalars_ref[2 * slots + step]).astype(jnp.bfloat16)

        @pl.when(step == 0)
        def _():
            out_ref[...] = amplitude.astype(jnp.float32)

        @pl.when(step > 0)
        def _():
            out_ref[...] += amplitude.astype(jnp.float32)

    @pl.when(tiles_ref[step] == 0)
    def _():
        accumulate(mine_ref)

    @pl.when(tiles_ref[step] != 0)
    def _():
        accumulate(theirs_ref)


def held_index(present, local):
    steps = jnp.arange(present.shape[0], dtype=jnp.int32)
    last = lax.cummax(jnp.where(present, steps, -1))
    first = jnp.argmax(present)
    return jnp.where(last >= 0, local[jnp.maximum(last, 0)], local[first])


def summed_tiles(position, scalars, mine, theirs, column, pair_sum):
    slots = position.shape[0]
    per_source = slots // column.shape[0]
    half, rows, depth = mine.shape
    in_theirs = position >= half
    local = position % half
    tables = jnp.concatenate(
        [in_theirs.astype(jnp.int32), held_index(~in_theirs, local), held_index(in_theirs, local)]
    )
    grid_spec = pltpu.PrefetchScalarGridSpec(
        num_scalar_prefetch=1,
        grid=(slots,),
        in_specs=[
            pl.BlockSpec(memory_space=pltpu.SMEM),
            pl.BlockSpec((None, rows, depth), lambda s, tiles: (tiles[slots + s], 0, 0)),
            pl.BlockSpec((None, rows, depth), lambda s, tiles: (tiles[2 * slots + s], 0, 0)),
            pl.BlockSpec((None, depth, rows), lambda s, tiles: (s // per_source, 0, 0)),
            pl.BlockSpec((rows, rows), lambda s, tiles: (0, 0)),
        ],
        out_specs=pl.BlockSpec((rows, rows), lambda s, tiles: (0, 0)),
    )
    return pl.pallas_call(
        slot_kernel,
        grid_spec=grid_spec,
        out_shape=jax.ShapeDtypeStruct((rows, rows), jnp.float32),
        compiler_params=pltpu.CompilerParams(dimension_semantics=("arbitrary",)),
    )(tables, scalars, mine, theirs, column, pair_sum)


def layer(df_panels, occ_energy, virt_energy, fock_off, i_plan, pair_owner, pair_weight):
    highest = lax.Precision.HIGHEST
    halves = lax.axis_size("zh")
    cores = lax.axis_size("core")
    group_count = halves * cores
    orbit_count = lax.axis_size("orb")
    my_core = lax.axis_index("core")
    my_group = lax.axis_index("zh") * cores + my_core
    my_index = lax.axis_index("orb")
    my_orbital = my_group * orbit_count + my_index
    own_panel = df_panels[0]
    tile_count = STEPS * group_count

    groups_range = jnp.arange(group_count, dtype=jnp.int32)
    i_ids = (groups_range[None, :] * orbit_count + i_plan).reshape(tile_count)
    own_turned = own_panel.T
    core_ids = lax.dynamic_index_in_dim(
        i_ids.reshape(STEPS, halves, cores), my_core, axis=2, keepdims=False
    ).reshape(-1)
    masked = jnp.where(
        (core_ids == my_orbital)[:, None, None], own_turned[None], jnp.zeros((), own_panel.dtype)
    )
    own_half = lax.psum(masked, ("zh", "orb"))
    other_half = lax.ppermute(own_half, "core", [(c, c ^ 1) for c in range(cores)])

    meta = jnp.concatenate([pair_weight, pair_owner[:, 0].astype(jnp.float32)])
    across = [(z, z ^ 1) for z in range(halves)]
    beside = [(c, c ^ 1) for c in range(cores)]
    far_panel = lax.ppermute(own_panel, "zh", across)
    far_meta = lax.ppermute(meta, "zh", across)
    near = lax.ppermute(jnp.stack([own_panel, far_panel]), "core", beside)
    near_meta = lax.ppermute(jnp.stack([meta, far_meta]), "core", beside)
    column = jnp.stack([own_panel, far_panel, near[0], near[1]])
    column_meta = jnp.stack([meta, far_meta, near_meta[0], near_meta[1]])
    source_groups = jnp.stack([my_group, my_group ^ 2, my_group ^ 1, my_group ^ 3])

    weights = column_meta[:, :tile_count]
    owners = column_meta[:, tile_count:]
    mine = owners == my_group.astype(jnp.float32)
    rank = jnp.cumsum(mine.astype(jnp.int32), axis=1) - 1
    slot_hit = mine[:, None, :] & (rank[:, None, :] == jnp.arange(CAP)[None, :, None])
    tile_range = jnp.arange(tile_count, dtype=jnp.int32)
    slot_tile = jnp.sum(jnp.where(slot_hit, tile_range, 0), axis=2)
    slot_weight = jnp.sum(jnp.where(slot_hit, weights[:, None, :], 0.0), axis=2)

    pair_sum = virt_energy[:, None] + virt_energy[None, :]
    i_energy = occ_energy[i_ids][slot_tile]
    j_energy = occ_energy[source_groups * orbit_count + my_index]
    scalars = jnp.concatenate(
        [
            i_energy.reshape(-1),
            jnp.repeat(j_energy, CAP),
            slot_weight.reshape(-1),
        ]
    )
    step_of, group_of = slot_tile // group_count, slot_tile % group_count
    position = (
        jnp.where(group_of % cores == my_core, 0, tile_count // cores)
        + step_of * halves
        + group_of // cores
    )
    summed = summed_tiles(position.reshape(-1), scalars, own_half, other_half, column, pair_sum)

    fock_matrix = jnp.diag(virt_energy) + 0.5 * (fock_off + fock_off.T)
    paired = jnp.dot(
        jnp.concatenate([fock_matrix, summed], axis=1),
        jnp.concatenate([summed, fock_matrix], axis=0),
        precision=highest,
    )
    return paired[None]


def solution(mesh):
    group_count, orbit_count = mesh.devices.shape
    split = Mesh(mesh.devices.reshape(2, group_count // 2, orbit_count), ("zh", "core", "orb"))
    spread = ("zh", "core", "orb")
    placed = (
        P(spread, None, None),
        P(),
        P(),
        P(),
        P(),
        P(spread, None),
        P(spread),
    )
    return jax.shard_map(
        layer, mesh=split, in_specs=placed, out_specs=P(spread, None, None), check_vma=False
    )
```

```python
import jax
import jax.numpy as jnp
from jax import lax
from jax.sharding import Mesh, PartitionSpec as P
from jax.experimental import pallas as pl
from jax.experimental.pallas import tpu as pltpu

STEPS = 3
CAP = 4


def slot_kernel(tiles_ref, scalars_ref, mine_ref, theirs_ref, right_ref, pair_ref, out_ref):
    step = pl.program_id(0)
    slots = pl.num_programs(0)

    def accumulate(left_ref):
        band = left_ref.shape[0] // 2
        for lo in (0, band):
            rows = pl.ds(lo, band)
            integral = jnp.dot(left_ref[rows, :], right_ref[...], preferred_element_type=jnp.float32)
            denominator = (pair_ref[rows, :] - scalars_ref[step]) - scalars_ref[slots + step]
            scaled = (integral / denominator) * scalars_ref[2 * slots + step]
            amplitude = scaled.astype(jnp.bfloat16).astype(jnp.float32)

            @pl.when(step == 0)
            def _():
                out_ref[rows, :] = amplitude

            @pl.when(step > 0)
            def _():
                out_ref[rows, :] += amplitude

    @pl.when(tiles_ref[step] == 0)
    def _():
        accumulate(mine_ref)

    @pl.when(tiles_ref[step] != 0)
    def _():
        accumulate(theirs_ref)


def held_index(present, local):
    steps = jnp.arange(present.shape[0], dtype=jnp.int32)
    last = lax.cummax(jnp.where(present, steps, -1))
    first = jnp.argmax(present)
    return jnp.where(last >= 0, local[jnp.maximum(last, 0)], local[first])


def summed_tiles(position, scalars, mine, theirs, column, pair_sum):
    slots = position.shape[0]
    per_source = slots // column.shape[0]
    half, rows, depth = mine.shape
    in_theirs = position >= half
    local = position % half
    tables = jnp.concatenate(
        [in_theirs.astype(jnp.int32), held_index(~in_theirs, local), held_index(in_theirs, local)]
    )
    grid_spec = pltpu.PrefetchScalarGridSpec(
        num_scalar_prefetch=1,
        grid=(slots,),
        in_specs=[
            pl.BlockSpec(memory_space=pltpu.SMEM),
            pl.BlockSpec((None, rows, depth), lambda s, tiles: (tiles[slots + s], 0, 0)),
            pl.BlockSpec((None, rows, depth), lambda s, tiles: (tiles[2 * slots + s], 0, 0)),
            pl.BlockSpec((None, depth, rows), lambda s, tiles: (s // per_source, 0, 0)),
            pl.BlockSpec((rows, rows), lambda s, tiles: (0, 0)),
        ],
        out_specs=pl.BlockSpec((rows, rows), lambda s, tiles: (0, 0)),
    )
    return pl.pallas_call(
        slot_kernel,
        grid_spec=grid_spec,
        out_shape=jax.ShapeDtypeStruct((rows, rows), jnp.float32),
        compiler_params=pltpu.CompilerParams(dimension_semantics=("arbitrary",)),
    )(tables, scalars, mine, theirs, column, pair_sum)


def layer(df_panels, occ_energy, virt_energy, fock_off, i_plan, pair_owner, pair_weight):
    highest = lax.Precision.HIGHEST
    halves = lax.axis_size("zh")
    cores = lax.axis_size("core")
    group_count = halves * cores
    orbit_count = lax.axis_size("orb")
    my_core = lax.axis_index("core")
    my_group = lax.axis_index("zh") * cores + my_core
    my_index = lax.axis_index("orb")
    my_orbital = my_group * orbit_count + my_index
    own_panel = df_panels[0]
    tile_count = STEPS * group_count

    groups_range = jnp.arange(group_count, dtype=jnp.int32)
    i_ids = (groups_range[None, :] * orbit_count + i_plan).reshape(tile_count)
    own_turned = own_panel.T
    core_ids = lax.dynamic_index_in_dim(
        i_ids.reshape(STEPS, halves, cores), my_core, axis=2, keepdims=False
    ).reshape(-1)
    masked = jnp.where(
        (core_ids == my_orbital)[:, None, None], own_turned[None], jnp.zeros((), own_panel.dtype)
    )
    own_half = lax.psum(masked, ("zh", "orb"))
    other_half = lax.ppermute(own_half, "core", [(c, c ^ 1) for c in range(cores)])

    meta = jnp.concatenate([pair_weight, pair_owner[:, 0].astype(jnp.float32)])
    across = [(z, z ^ 1) for z in range(halves)]
    beside = [(c, c ^ 1) for c in range(cores)]
    far_panel = lax.ppermute(own_panel, "zh", across)
    far_meta = lax.ppermute(meta, "zh", across)
    near = lax.ppermute(jnp.stack([own_panel, far_panel]), "core", beside)
    near_meta = lax.ppermute(jnp.stack([meta, far_meta]), "core", beside)
    column = jnp.stack([own_panel, far_panel, near[0], near[1]])
    column_meta = jnp.stack([meta, far_meta, near_meta[0], near_meta[1]])
    source_groups = jnp.stack([my_group, my_group ^ 2, my_group ^ 1, my_group ^ 3])

    weights = column_meta[:, :tile_count]
    owners = column_meta[:, tile_count:]
    mine = owners == my_group.astype(jnp.float32)
    rank = jnp.cumsum(mine.astype(jnp.int32), axis=1) - 1
    slot_hit = mine[:, None, :] & (rank[:, None, :] == jnp.arange(CAP)[None, :, None])
    tile_range = jnp.arange(tile_count, dtype=jnp.int32)
    slot_tile = jnp.sum(jnp.where(slot_hit, tile_range, 0), axis=2)
    slot_weight = jnp.sum(jnp.where(slot_hit, weights[:, None, :], 0.0), axis=2)

    pair_sum = virt_energy[:, None] + virt_energy[None, :]
    i_energy = occ_energy[i_ids][slot_tile]
    j_energy = occ_energy[source_groups * orbit_count + my_index]
    scalars = jnp.concatenate(
        [
            i_energy.reshape(-1),
            jnp.repeat(j_energy, CAP),
            slot_weight.reshape(-1),
        ]
    )
    step_of, group_of = slot_tile // group_count, slot_tile % group_count
    position = (
        jnp.where(group_of % cores == my_core, 0, tile_count // cores)
        + step_of * halves
        + group_of // cores
    )
    summed = summed_tiles(position.reshape(-1), scalars, own_half, other_half, column, pair_sum)

    fock_matrix = jnp.diag(virt_energy) + 0.5 * (fock_off + fock_off.T)
    left = jnp.dot(fock_matrix, summed, precision=highest)
    right = jnp.dot(summed, fock_matrix, precision=highest)
    return (left + right)[None]


def solution(mesh):
    group_count, orbit_count = mesh.devices.shape
    split = Mesh(mesh.devices.reshape(2, group_count // 2, orbit_count), ("zh", "core", "orb"))
    spread = ("zh", "core", "orb")
    placed = (
        P(spread, None, None),
        P(),
        P(),
        P(),
        P(),
        P(spread, None),
        P(spread),
    )
    return jax.shard_map(
        layer, mesh=split, in_specs=placed, out_specs=P(spread, None, None), check_vma=False
    )
```

```python
import jax
import jax.numpy as jnp
from jax import lax
from jax.sharding import Mesh, PartitionSpec as P
from jax.experimental import pallas as pl
from jax.experimental.pallas import tpu as pltpu

STEPS = 3
CAP = 4


def slot_kernel(tiles_ref, scalars_ref, *refs):
    *lefts, right_ref, pair_ref, out_ref = refs
    step = pl.program_id(0)
    steps = pl.num_programs(0)
    streams = len(lefts) // 2
    slots = streams * steps
    total = None
    for stream in range(streams):
        slot = streams * step + stream
        mine_ref, theirs_ref = lefts[2 * stream], lefts[2 * stream + 1]
        from_theirs = tiles_ref[3 * stream * steps + step] != 0
        left = jnp.where(from_theirs, theirs_ref[...], mine_ref[...])
        integral = jnp.dot(left, right_ref[...], preferred_element_type=jnp.float32)
        denominator = (pair_ref[...] - scalars_ref[slot]) - scalars_ref[slots + slot]
        scaled = (integral / denominator) * scalars_ref[2 * slots + slot]
        amplitude = scaled.astype(jnp.bfloat16).astype(jnp.float32)
        total = amplitude if total is None else total + amplitude

    @pl.when(step == 0)
    def _():
        out_ref[...] = total

    @pl.when(step > 0)
    def _():
        out_ref[...] += total


def held_index(present, local):
    steps = jnp.arange(present.shape[0], dtype=jnp.int32)
    last = lax.cummax(jnp.where(present, steps, -1))
    first = jnp.argmax(present)
    return jnp.where(last >= 0, local[jnp.maximum(last, 0)], local[first])


def summed_tiles(position, scalars, mine, theirs, column, pair_sum):
    slots = position.shape[0]
    streams = 4
    steps = slots // streams
    per_source = slots // column.shape[0]
    half, rows, depth = mine.shape
    parts = []
    for stream in range(streams):
        picked = position[stream::streams]
        in_theirs = picked >= half
        local = picked % half
        parts += [
            in_theirs.astype(jnp.int32),
            held_index(~in_theirs, local),
            held_index(in_theirs, local),
        ]
    tables = jnp.concatenate(parts)

    def left_spec(stream, kind):
        offset = (3 * stream + kind) * steps
        return pl.BlockSpec((None, rows, depth), lambda p, tiles: (tiles[offset + p], 0, 0))

    grid_spec = pltpu.PrefetchScalarGridSpec(
        num_scalar_prefetch=1,
        grid=(steps,),
        in_specs=[pl.BlockSpec(memory_space=pltpu.SMEM)]
        + [left_spec(stream, kind) for stream in range(streams) for kind in (1, 2)]
        + [
            pl.BlockSpec((None, depth, rows), lambda p, tiles: (p * streams // per_source, 0, 0)),
            pl.BlockSpec((rows, rows), lambda p, tiles: (0, 0)),
        ],
        out_specs=pl.BlockSpec((rows, rows), lambda p, tiles: (0, 0)),
    )
    lefts = [mine, theirs] * streams
    return pl.pallas_call(
        slot_kernel,
        grid_spec=grid_spec,
        out_shape=jax.ShapeDtypeStruct((rows, rows), jnp.float32),
        compiler_params=pltpu.CompilerParams(dimension_semantics=("arbitrary",)),
    )(tables, scalars, *lefts, column, pair_sum)


def layer(df_panels, occ_energy, virt_energy, fock_off, i_plan, pair_owner, pair_weight):
    highest = lax.Precision.HIGHEST
    halves = lax.axis_size("zh")
    cores = lax.axis_size("core")
    group_count = halves * cores
    orbit_count = lax.axis_size("orb")
    my_core = lax.axis_index("core")
    my_group = lax.axis_index("zh") * cores + my_core
    my_index = lax.axis_index("orb")
    my_orbital = my_group * orbit_count + my_index
    own_panel = df_panels[0]
    tile_count = STEPS * group_count

    groups_range = jnp.arange(group_count, dtype=jnp.int32)
    i_ids = (groups_range[None, :] * orbit_count + i_plan).reshape(tile_count)
    own_turned = own_panel.T
    core_ids = lax.dynamic_index_in_dim(
        i_ids.reshape(STEPS, halves, cores), my_core, axis=2, keepdims=False
    ).reshape(-1)
    masked = jnp.where(
        (core_ids == my_orbital)[:, None, None], own_turned[None], jnp.zeros((), own_panel.dtype)
    )
    own_half = lax.psum(masked, ("zh", "orb"))
    other_half = lax.ppermute(own_half, "core", [(c, c ^ 1) for c in range(cores)])

    meta = jnp.concatenate([pair_weight, pair_owner[:, 0].astype(jnp.float32)])
    across = [(z, z ^ 1) for z in range(halves)]
    beside = [(c, c ^ 1) for c in range(cores)]
    far_panel = lax.ppermute(own_panel, "zh", across)
    far_meta = lax.ppermute(meta, "zh", across)
    near = lax.ppermute(jnp.stack([own_panel, far_panel]), "core", beside)
    near_meta = lax.ppermute(jnp.stack([meta, far_meta]), "core", beside)
    column = jnp.stack([own_panel, far_panel, near[0], near[1]])
    column_meta = jnp.stack([meta, far_meta, near_meta[0], near_meta[1]])
    source_groups = jnp.stack([my_group, my_group ^ 2, my_group ^ 1, my_group ^ 3])

    weights = column_meta[:, :tile_count]
    owners = column_meta[:, tile_count:]
    mine = owners == my_group.astype(jnp.float32)
    rank = jnp.cumsum(mine.astype(jnp.int32), axis=1) - 1
    slot_hit = mine[:, None, :] & (rank[:, None, :] == jnp.arange(CAP)[None, :, None])
    tile_range = jnp.arange(tile_count, dtype=jnp.int32)
    slot_tile = jnp.sum(jnp.where(slot_hit, tile_range, 0), axis=2)
    slot_weight = jnp.sum(jnp.where(slot_hit, weights[:, None, :], 0.0), axis=2)

    pair_sum = virt_energy[:, None] + virt_energy[None, :]
    i_energy = occ_energy[i_ids][slot_tile]
    j_energy = occ_energy[source_groups * orbit_count + my_index]
    scalars = jnp.concatenate(
        [
            i_energy.reshape(-1),
            jnp.repeat(j_energy, CAP),
            slot_weight.reshape(-1),
        ]
    )
    step_of, group_of = slot_tile // group_count, slot_tile % group_count
    position = (
        jnp.where(group_of % cores == my_core, 0, tile_count // cores)
        + step_of * halves
        + group_of // cores
    )
    summed = summed_tiles(position.reshape(-1), scalars, own_half, other_half, column, pair_sum)

    fock_matrix = jnp.diag(virt_energy) + 0.5 * (fock_off + fock_off.T)
    left = jnp.dot(fock_matrix, summed, precision=highest)
    right = jnp.dot(summed, fock_matrix, precision=highest)
    return (left + right)[None]


def solution(mesh):
    group_count, orbit_count = mesh.devices.shape
    split = Mesh(mesh.devices.reshape(2, group_count // 2, orbit_count), ("zh", "core", "orb"))
    spread = ("zh", "core", "orb")
    placed = (
        P(spread, None, None),
        P(),
        P(),
        P(),
        P(),
        P(spread, None),
        P(spread),
    )
    return jax.shard_map(
        layer, mesh=split, in_specs=placed, out_specs=P(spread, None, None), check_vma=False
    )
```

```python
import jax
import jax.numpy as jnp
from jax import lax
from jax.sharding import Mesh, PartitionSpec as P
from jax.experimental import pallas as pl
from jax.experimental.pallas import tpu as pltpu

STEPS = 3
CAP = 4


def slot_kernel(tiles_ref, scalars_ref, *refs):
    *lefts, right_ref, pair_ref, out_ref = refs
    step = pl.program_id(0)
    steps = pl.num_programs(0)
    streams = len(lefts) // 2
    slots = streams * steps
    total = None
    for stream in range(streams):
        slot = streams * step + stream
        mine_ref, theirs_ref = lefts[2 * stream], lefts[2 * stream + 1]
        from_theirs = tiles_ref[3 * stream * steps + step] != 0
        left = jnp.where(from_theirs, theirs_ref[...], mine_ref[...])
        integral = jnp.dot(left, right_ref[...], preferred_element_type=jnp.float32)
        denominator = (pair_ref[...] - scalars_ref[slot]) - scalars_ref[slots + slot]
        scaled = (integral / denominator) * scalars_ref[2 * slots + slot]
        amplitude = scaled.astype(jnp.bfloat16).astype(jnp.float32)
        total = amplitude if total is None else total + amplitude

    @pl.when(step == 0)
    def _():
        out_ref[...] = total

    @pl.when(step > 0)
    def _():
        out_ref[...] += total


def held_index(present, local):
    steps = jnp.arange(present.shape[0], dtype=jnp.int32)
    last = lax.cummax(jnp.where(present, steps, -1))
    first = jnp.argmax(present)
    return jnp.where(last >= 0, local[jnp.maximum(last, 0)], local[first])


def summed_tiles(position, scalars, mine, theirs, column, pair_sum):
    slots = position.shape[0]
    streams = 2
    steps = slots // streams
    per_source = slots // column.shape[0]
    half, rows, depth = mine.shape
    parts = []
    for stream in range(streams):
        picked = position[stream::streams]
        in_theirs = picked >= half
        local = picked % half
        parts += [
            in_theirs.astype(jnp.int32),
            held_index(~in_theirs, local),
            held_index(in_theirs, local),
        ]
    tables = jnp.concatenate(parts)

    def left_spec(stream, kind):
        offset = (3 * stream + kind) * steps
        return pl.BlockSpec((None, rows, depth), lambda p, tiles: (tiles[offset + p], 0, 0))

    grid_spec = pltpu.PrefetchScalarGridSpec(
        num_scalar_prefetch=1,
        grid=(steps,),
        in_specs=[pl.BlockSpec(memory_space=pltpu.SMEM)]
        + [left_spec(stream, kind) for stream in range(streams) for kind in (1, 2)]
        + [
            pl.BlockSpec((None, depth, rows), lambda p, tiles: (p * streams // per_source, 0, 0)),
            pl.BlockSpec((rows, rows), lambda p, tiles: (0, 0)),
        ],
        out_specs=pl.BlockSpec((rows, rows), lambda p, tiles: (0, 0)),
    )
    lefts = [mine, theirs] * streams
    return pl.pallas_call(
        slot_kernel,
        grid_spec=grid_spec,
        out_shape=jax.ShapeDtypeStruct((rows, rows), jnp.float32),
        compiler_params=pltpu.CompilerParams(dimension_semantics=("arbitrary",)),
    )(tables, scalars, *lefts, column, pair_sum)


def layer(df_panels, occ_energy, virt_energy, fock_off, i_plan, pair_owner, pair_weight):
    halves = lax.axis_size("zh")
    cores = lax.axis_size("core")
    group_count = halves * cores
    orbit_count = lax.axis_size("orb")
    my_core = lax.axis_index("core")
    my_group = lax.axis_index("zh") * cores + my_core
    my_index = lax.axis_index("orb")
    my_orbital = my_group * orbit_count + my_index
    own_panel = df_panels[0]
    tile_count = STEPS * group_count

    groups_range = jnp.arange(group_count, dtype=jnp.int32)
    i_ids = (groups_range[None, :] * orbit_count + i_plan).reshape(tile_count)
    own_turned = own_panel.T
    core_ids = lax.dynamic_index_in_dim(
        i_ids.reshape(STEPS, halves, cores), my_core, axis=2, keepdims=False
    ).reshape(-1)
    masked = jnp.where(
        (core_ids == my_orbital)[:, None, None], own_turned[None], jnp.zeros((), own_panel.dtype)
    )
    own_half = lax.psum(masked, ("zh", "orb"))
    other_half = lax.ppermute(own_half, "core", [(c, c ^ 1) for c in range(cores)])

    meta = jnp.concatenate([pair_weight, pair_owner[:, 0].astype(jnp.float32)])
    across = [(z, z ^ 1) for z in range(halves)]
    beside = [(c, c ^ 1) for c in range(cores)]
    far_panel = lax.ppermute(own_panel, "zh", across)
    far_meta = lax.ppermute(meta, "zh", across)
    near = lax.ppermute(jnp.stack([own_panel, far_panel]), "core", beside)
    near_meta = lax.ppermute(jnp.stack([meta, far_meta]), "core", beside)
    column = jnp.stack([own_panel, far_panel, near[0], near[1]])
    column_meta = jnp.stack([meta, far_meta, near_meta[0], near_meta[1]])
    source_groups = jnp.stack([my_group, my_group ^ 2, my_group ^ 1, my_group ^ 3])

    weights = column_meta[:, :tile_count]
    owners = column_meta[:, tile_count:]
    mine = owners == my_group.astype(jnp.float32)
    rank = jnp.cumsum(mine.astype(jnp.int32), axis=1) - 1
    slot_hit = mine[:, None, :] & (rank[:, None, :] == jnp.arange(CAP)[None, :, None])
    tile_range = jnp.arange(tile_count, dtype=jnp.int32)
    slot_tile = jnp.sum(jnp.where(slot_hit, tile_range, 0), axis=2)
    slot_weight = jnp.sum(jnp.where(slot_hit, weights[:, None, :], 0.0), axis=2)

    pair_sum = virt_energy[:, None] + virt_energy[None, :]
    i_energy = occ_energy[i_ids][slot_tile]
    j_energy = occ_energy[source_groups * orbit_count + my_index]
    scalars = jnp.concatenate(
        [
            i_energy.reshape(-1),
            jnp.repeat(j_energy, CAP),
            slot_weight.reshape(-1),
        ]
    )
    step_of, group_of = slot_tile // group_count, slot_tile % group_count
    position = (
        jnp.where(group_of % cores == my_core, 0, tile_count // cores)
        + step_of * halves
        + group_of // cores
    )
    summed = summed_tiles(position.reshape(-1), scalars, own_half, other_half, column, pair_sum)

    fock_matrix = jnp.diag(virt_energy) + 0.5 * (fock_off + fock_off.T)

    def split(value):
        high = value.astype(jnp.bfloat16)
        return high, (value - high.astype(jnp.float32)).astype(jnp.bfloat16)

    fock_high, fock_low = split(fock_matrix)
    sum_high, sum_low = split(summed)

    def product(a, b):
        return jnp.dot(a, b, preferred_element_type=jnp.float32)

    left = product(fock_high, sum_high) + (product(fock_high, sum_low) + product(fock_low, sum_high))
    right = product(sum_high, fock_high) + (product(sum_high, fock_low) + product(sum_low, fock_high))
    return (left + right)[None]


def solution(mesh):
    group_count, orbit_count = mesh.devices.shape
    split = Mesh(mesh.devices.reshape(2, group_count // 2, orbit_count), ("zh", "core", "orb"))
    spread = ("zh", "core", "orb")
    placed = (
        P(spread, None, None),
        P(),
        P(),
        P(),
        P(),
        P(spread, None),
        P(spread),
    )
    return jax.shard_map(
        layer, mesh=split, in_specs=placed, out_specs=P(spread, None, None), check_vma=False
    )
```

```python
import jax
import jax.numpy as jnp
from jax import lax
from jax.sharding import Mesh, PartitionSpec as P
from jax.experimental import pallas as pl
from jax.experimental.pallas import tpu as pltpu

STEPS = 3
CAP = 4


def slot_kernel(tiles_ref, scalars_ref, *refs):
    *lefts, right_ref, pair_ref, out_ref = refs
    step = pl.program_id(0)
    steps = pl.num_programs(0)
    streams = len(lefts) // 2
    slots = streams * steps
    total = None
    for stream in range(streams):
        slot = streams * step + stream
        mine_ref, theirs_ref = lefts[2 * stream], lefts[2 * stream + 1]
        from_theirs = tiles_ref[3 * stream * steps + step] != 0
        left = jnp.where(from_theirs, theirs_ref[...], mine_ref[...])
        integral = lax.dot_general(
            left, right_ref[...], (((0,), (0,)), ((), ())), preferred_element_type=jnp.float32
        )
        denominator = (pair_ref[...] - scalars_ref[slot]) - scalars_ref[slots + slot]
        scaled = (integral / denominator) * scalars_ref[2 * slots + slot]
        amplitude = scaled.astype(jnp.bfloat16).astype(jnp.float32)
        total = amplitude if total is None else total + amplitude

    @pl.when(step == 0)
    def _():
        out_ref[...] = total

    @pl.when(step > 0)
    def _():
        out_ref[...] += total


def held_index(present, local):
    steps = jnp.arange(present.shape[0], dtype=jnp.int32)
    last = lax.cummax(jnp.where(present, steps, -1))
    first = jnp.argmax(present)
    return jnp.where(last >= 0, local[jnp.maximum(last, 0)], local[first])


def summed_tiles(position, scalars, mine, theirs, column, pair_sum):
    slots = position.shape[0]
    streams = 2
    steps = slots // streams
    per_source = slots // column.shape[0]
    half, depth, rows = mine.shape
    parts = []
    for stream in range(streams):
        picked = position[stream::streams]
        in_theirs = picked >= half
        local = picked % half
        parts += [
            in_theirs.astype(jnp.int32),
            held_index(~in_theirs, local),
            held_index(in_theirs, local),
        ]
    tables = jnp.concatenate(parts)

    def left_spec(stream, kind):
        offset = (3 * stream + kind) * steps
        return pl.BlockSpec((None, depth, rows), lambda p, tiles: (tiles[offset + p], 0, 0))

    grid_spec = pltpu.PrefetchScalarGridSpec(
        num_scalar_prefetch=1,
        grid=(steps,),
        in_specs=[pl.BlockSpec(memory_space=pltpu.SMEM)]
        + [left_spec(stream, kind) for stream in range(streams) for kind in (1, 2)]
        + [
            pl.BlockSpec((None, depth, rows), lambda p, tiles: (p * streams // per_source, 0, 0)),
            pl.BlockSpec((rows, rows), lambda p, tiles: (0, 0)),
        ],
        out_specs=pl.BlockSpec((rows, rows), lambda p, tiles: (0, 0)),
    )
    lefts = [mine, theirs] * streams
    return pl.pallas_call(
        slot_kernel,
        grid_spec=grid_spec,
        out_shape=jax.ShapeDtypeStruct((rows, rows), jnp.float32),
        compiler_params=pltpu.CompilerParams(dimension_semantics=("arbitrary",)),
    )(tables, scalars, *lefts, column, pair_sum)


def layer(df_panels, occ_energy, virt_energy, fock_off, i_plan, pair_owner, pair_weight):
    highest = lax.Precision.HIGHEST
    halves = lax.axis_size("zh")
    cores = lax.axis_size("core")
    group_count = halves * cores
    orbit_count = lax.axis_size("orb")
    my_core = lax.axis_index("core")
    my_group = lax.axis_index("zh") * cores + my_core
    my_index = lax.axis_index("orb")
    my_orbital = my_group * orbit_count + my_index
    own_panel = df_panels[0]
    tile_count = STEPS * group_count

    groups_range = jnp.arange(group_count, dtype=jnp.int32)
    i_ids = (groups_range[None, :] * orbit_count + i_plan).reshape(tile_count)
    core_ids = lax.dynamic_index_in_dim(
        i_ids.reshape(STEPS, halves, cores), my_core, axis=2, keepdims=False
    ).reshape(-1)
    masked = jnp.where(
        (core_ids == my_orbital)[:, None, None], own_panel[None], jnp.zeros((), own_panel.dtype)
    )
    own_half = lax.psum(masked, ("zh", "orb"))
    other_half = lax.ppermute(own_half, "core", [(c, c ^ 1) for c in range(cores)])

    meta = jnp.concatenate([pair_weight, pair_owner[:, 0].astype(jnp.float32)])
    across = [(z, z ^ 1) for z in range(halves)]
    beside = [(c, c ^ 1) for c in range(cores)]
    far_panel = lax.ppermute(own_panel, "zh", across)
    far_meta = lax.ppermute(meta, "zh", across)
    near = lax.ppermute(jnp.stack([own_panel, far_panel]), "core", beside)
    near_meta = lax.ppermute(jnp.stack([meta, far_meta]), "core", beside)
    column = jnp.stack([own_panel, far_panel, near[0], near[1]])
    column_meta = jnp.stack([meta, far_meta, near_meta[0], near_meta[1]])
    source_groups = jnp.stack([my_group, my_group ^ 2, my_group ^ 1, my_group ^ 3])

    weights = column_meta[:, :tile_count]
    owners = column_meta[:, tile_count:]
    mine = owners == my_group.astype(jnp.float32)
    rank = jnp.cumsum(mine.astype(jnp.int32), axis=1) - 1
    slot_hit = mine[:, None, :] & (rank[:, None, :] == jnp.arange(CAP)[None, :, None])
    tile_range = jnp.arange(tile_count, dtype=jnp.int32)
    slot_tile = jnp.sum(jnp.where(slot_hit, tile_range, 0), axis=2)
    slot_weight = jnp.sum(jnp.where(slot_hit, weights[:, None, :], 0.0), axis=2)

    pair_sum = virt_energy[:, None] + virt_energy[None, :]
    i_energy = occ_energy[i_ids][slot_tile]
    j_energy = occ_energy[source_groups * orbit_count + my_index]
    scalars = jnp.concatenate(
        [
            i_energy.reshape(-1),
            jnp.repeat(j_energy, CAP),
            slot_weight.reshape(-1),
        ]
    )
    step_of, group_of = slot_tile // group_count, slot_tile % group_count
    position = (
        jnp.where(group_of % cores == my_core, 0, tile_count // cores)
        + step_of * halves
        + group_of // cores
    )
    summed = summed_tiles(position.reshape(-1), scalars, own_half, other_half, column, pair_sum)

    fock_matrix = jnp.diag(virt_energy) + 0.5 * (fock_off + fock_off.T)
    left = jnp.dot(fock_matrix, summed, precision=highest)
    right = jnp.dot(summed, fock_matrix, precision=highest)
    return (left + right)[None]


def solution(mesh):
    group_count, orbit_count = mesh.devices.shape
    split = Mesh(mesh.devices.reshape(2, group_count // 2, orbit_count), ("zh", "core", "orb"))
    spread = ("zh", "core", "orb")
    placed = (
        P(spread, None, None),
        P(),
        P(),
        P(),
        P(),
        P(spread, None),
        P(spread),
    )
    return jax.shard_map(
        layer, mesh=split, in_specs=placed, out_specs=P(spread, None, None), check_vma=False
    )
```
